256 devices in a mesh: scene: 16 (over y, z_hi), seq: 16 (over z_lo, x, core).
Axes of the slice: x: 4, y: 4, z: 8 (z_hi: 4, z_lo: 2; z = z_hi * 2 + z_lo), core: 2. Of those that a mesh axis runs over, the one named last changes fastest.
Arguments:
- scene_x: bfloat16 [16, 65536, 256], P('scene', 'seq'), may hold values from -6 to 6
- cotangent: bfloat16 [16, 65536, 256], P('scene', 'seq'), may hold values from -6 to 6
- gate_gain: float32 [256], replicated, may hold values from 0.3 to 3
- kernel: bfloat16 [256, 256, 256], P(None, 'seq'), may hold values from -6 to 6
- block_mix: bfloat16 [256, 256], replicated, may hold values from -0.375 to 0.375
- across_mix: bfloat16 [256, 256], replicated, may hold values from -0.375 to 0.375
- across_unmix: bfloat16 [256, 256], replicated, may hold values from -0.375 to 0.375
- block_unmix: bfloat16 [256, 256], replicated, may hold values from -0.375 to 0.375
Outputs:
- mixed: bfloat16 [16, 65536, 256], P('scene', 'seq')
- grad_x: bfloat16 [16, 65536, 256], P('scene', 'seq')
- grad_kernel: float32 [256, 256, 256], P('scene', 'seq')
- grad_gain: float32 [256], replicated
The draws below stay inside these ranges and needn't reach their ends.
All inputs are finite; a program needn't handle non-finite values.
Results may differ from the reference program's by a relative error of at most 0.007.
Values may be sent and summed in bfloat16 or wider, within the bound.
No kernel may reach another device: no remote copies, remote signals or barrier semaphores. Data moves between devices by JAX's collectives and lax.ppermute only.
A program may use at most 128 MiB of HBM per device.

```python
import math
import jax
import jax.numpy as jnp
from jax import lax

A = 256
B = 256
D = 256
SCENES = 16
SEQLEN = 65536


def block_levels(key, shape, shards, low, high):
    gain = 1.0
    for position, parts in shards:
        draws = jax.random.uniform(jax.random.fold_in(jax.random.fold_in(key, 6), position), (parts,), jnp.float32, low / len(shards), high / len(shards))
        gain = gain * jnp.repeat(jnp.exp(draws), shape[position] // parts).reshape((-1,) + (1,) * (len(shape) - 1 - position))
    return gain


def noise(stream_key, shape, scale, limit, cuts=(), held_as=jnp.bfloat16):
    drawn = scale * jax.random.normal(stream_key, shape, jnp.float32)
    if cuts:
        drawn = drawn * block_levels(stream_key, shape, cuts, -0.22, 0.18)
    return jnp.clip(drawn, -limit, limit).astype(held_as)


def setup_inputs(seed: int = 0) -> dict:
    arg_keys = jax.random.split(jax.random.key(seed), 9)
    scene_x = noise(arg_keys[0], (SCENES, SEQLEN, D), 1.0, 6.0, ((0, 16), (1, 16)))
    cotangent = noise(arg_keys[1], (SCENES, SEQLEN, D), 1.0, 6.0, ((0, 16), (1, 16)))
    gate_gain = jnp.clip(jnp.exp(jax.random.uniform(arg_keys[2], (D,), jnp.float32, math.log(0.3), math.log(3.0))), 0.3, 3.0)
    kernel = noise(arg_keys[3], (A, B, D), 1.0, 6.0, ((1, 16),))
    block_mix = noise(arg_keys[4], (B, B), B ** -0.5, 0.375)
    across_mix = noise(arg_keys[5], (A, A), A ** -0.5, 0.375)
    across_unmix = noise(arg_keys[6], (A, A), A ** -0.5, 0.375)
    block_unmix = noise(arg_keys[7], (B, B), B ** -0.5, 0.375)
    return {"scene_x": scene_x, "cotangent": cotangent, "gate_gain": gate_gain, "kernel": kernel, "block_mix": block_mix, "across_mix": across_mix, "across_unmix": across_unmix, "block_unmix": block_unmix}


def one_scene(scene_rows, cotan_rows, gate_gain, kernel, block_mix, across_mix, across_unmix, block_unmix):
    f32 = jnp.float32
    bf16 = jnp.bfloat16
    inputs = scene_rows.astype(f32).reshape(A, B, D)
    kernel_f = kernel.astype(f32)
    first_f = block_mix.astype(f32)
    across_f = across_mix.astype(f32)
    unmix_f = across_unmix.astype(f32)
    last_f = block_unmix.astype(f32)
    first_mix = jnp.einsum('jb,abc->ajc', first_f, inputs).astype(bf16)
    second_mix = jnp.einsum('ia,ajc->ijc', across_f, first_mix.astype(f32)).astype(bf16)
    weighted = (second_mix.astype(f32) * kernel_f).astype(bf16)
    unmixed = jnp.einsum('pi,ijc->pjc', unmix_f, weighted.astype(f32)).astype(bf16)
    values = jnp.einsum('qj,pjc->pqc', last_f, unmixed.astype(f32))
    gate_pre = inputs * gate_gain
    gate_sig = jax.nn.sigmoid(gate_pre)
    mixed_out = (values * gate_pre * gate_sig).astype(bf16)
    upstream = cotan_rows.astype(f32).reshape(A, B, D)
    grad_values = (upstream * gate_pre * gate_sig).astype(bf16)
    grad_gate = upstream * values * gate_sig * (1.0 + gate_pre * (1.0 - gate_sig))
    grad_unmixed = jnp.einsum('qj,pqc->pjc', last_f, grad_values.astype(f32)).astype(bf16)
    grad_weighted = jnp.einsum('pi,pjc->ijc', unmix_f, grad_unmixed.astype(f32))
    kernel_term = grad_weighted * second_mix.astype(f32)
    grad_second = (grad_weighted * kernel_f).astype(bf16)
    grad_first = jnp.einsum('ia,ijc->ajc', across_f, grad_second.astype(f32)).astype(bf16)
    grad_input = jnp.einsum('jb,ajc->abc', first_f, grad_first.astype(f32)) + grad_gate * gate_gain
    gain_term = lax.optimization_barrier(jnp.sum(inputs * grad_gate, axis=(0, 1)))
    return (mixed_out.reshape(A * B, D), grad_input.astype(bf16).reshape(A * B, D), kernel_term, gain_term)

def reference(scene_x, cotangent, gate_gain, kernel, block_mix, across_mix, across_unmix, block_unmix):

    def step_scene(carry, pair):
        kernel_acc, gain_acc = carry
        mixed_out, grad_input, kernel_term, gain_term = one_scene(pair[0], pair[1], gate_gain, kernel, block_mix, across_mix, across_unmix, block_unmix)
        return ((kernel_acc + kernel_term, gain_acc + gain_term), (mixed_out, grad_input))
    start = (jnp.zeros((A, B, D), jnp.float32), jnp.zeros((D,), jnp.float32))
    (kernel_acc, gain_acc), (mixed, grad_x) = lax.scan(step_scene, start, (scene_x, cotangent))
    grad_scale = 1.0 / jnp.sqrt(jnp.float32(SCENES * A * B))
    return (mixed, grad_x, kernel_acc, gain_acc * grad_scale)
```

```python
import jax
import jax.numpy as jnp
from jax import lax
from jax.sharding import PartitionSpec as P


def on_device(
    scene_x, cotangent, gate_gain, kernel, block_mix, across_mix, across_unmix, block_unmix
):
    f32 = jnp.float32
    bf16 = jnp.bfloat16
    scenes_here, row_count, channels = scene_x.shape
    block_len = block_mix.shape[0]
    local_a = row_count // block_len
    parts = lax.axis_size("seq")
    chunk = block_len // parts
    kernel_f = kernel.astype(f32)

    inputs = scene_x.reshape(scenes_here, local_a, block_len, channels)
    upstream = cotangent.reshape(scenes_here, local_a, block_len, channels).astype(f32)
    gate_pre = inputs.astype(f32) * gate_gain
    gate_sig = jax.nn.sigmoid(gate_pre)
    gate = gate_pre * gate_sig
    grad_values = (upstream * gate).astype(bf16)
    mix_by_dest = block_mix.reshape(parts, chunk, block_len)
    unmix_by_dest = block_unmix.reshape(block_len, parts, chunk)
    first_mix = jnp.einsum(
        "Jjb,sabc->Jsajc", mix_by_dest, inputs, preferred_element_type=f32
    ).astype(bf16)
    grad_unmixed = jnp.einsum(
        "qJj,saqc->Jsajc", unmix_by_dest, grad_values, preferred_element_type=f32
    ).astype(bf16)
    outgoing = jnp.stack([first_mix, grad_unmixed], axis=1)
    incoming = lax.all_to_all(outgoing, "seq", split_axis=0, concat_axis=0, tiled=True)
    incoming = jnp.moveaxis(incoming, 2, 1)
    spread_mix = incoming[:, :, 0].reshape(parts, scenes_here, local_a, chunk, channels)
    spread_grad = incoming[:, :, 1].reshape(parts, scenes_here, local_a, chunk, channels)
    spread_mix = jnp.moveaxis(spread_mix, 1, 0).reshape(scenes_here, parts * local_a, chunk, channels)
    spread_grad = jnp.moveaxis(spread_grad, 1, 0).reshape(
        scenes_here, parts * local_a, chunk, channels
    )

    second_mix = jnp.einsum(
        "ia,sajc->sijc", across_mix, spread_mix, preferred_element_type=f32
    ).astype(bf16)
    weighted = (second_mix.astype(f32) * kernel_f).astype(bf16)
    unmixed = jnp.einsum(
        "pi,sijc->spjc", across_unmix, weighted, preferred_element_type=f32
    ).astype(bf16)
    grad_weighted = jnp.einsum(
        "pi,spjc->sijc", across_unmix, spread_grad, preferred_element_type=f32
    )
    kernel_term = jnp.sum(grad_weighted * second_mix.astype(f32), axis=0)
    kernel_grad = lax.psum_scatter(kernel_term, "scene", scatter_dimension=0, tiled=True)
    grad_second = (grad_weighted * kernel_f).astype(bf16)
    grad_first = jnp.einsum(
        "ia,sijc->sajc", across_mix, grad_second, preferred_element_type=f32
    ).astype(bf16)
    back = jnp.stack(
        [
            unmixed.reshape(scenes_here, parts, local_a, chunk, channels),
            grad_first.reshape(scenes_here, parts, local_a, chunk, channels),
        ],
        axis=2,
    )
    back = jnp.moveaxis(back, 1, 0)
    returned = lax.all_to_all(back, "seq", split_axis=0, concat_axis=0, tiled=True)
    values = jnp.einsum(
        "qJj,Jsajc->saqc",
        unmix_by_dest,
        returned[:, :, 0],
        preferred_element_type=f32,
    )
    mixed_out = (values * gate).astype(bf16).reshape(scenes_here, row_count, channels)
    grad_gate = upstream * values * gate_sig * (1.0 + gate_pre * (1.0 - gate_sig))
    grad_input = (
        jnp.einsum("Jjb,Jsajc->sabc", mix_by_dest, returned[:, :, 1], preferred_element_type=f32)
        + grad_gate * gate_gain
    )
    grad_input = grad_input.astype(bf16).reshape(scenes_here, row_count, channels)
    gain_term = jnp.sum(inputs.astype(f32) * grad_gate, axis=(0, 1, 2))
    gain_total = lax.psum(gain_term, ("scene", "seq"))
    total_rows = scenes_here * lax.axis_size("scene") * local_a * parts * block_len
    grad_scale = 1.0 / jnp.sqrt(jnp.float32(total_rows))
    return (mixed_out, grad_input, kernel_grad, gain_total * grad_scale)


def solution(mesh):
    return jax.shard_map(
        on_device,
        mesh=mesh,
        in_specs=(
            P("scene", "seq", None),
            P("scene", "seq", None),
            P(),
            P(None, "seq", None),
            P(),
            P(),
            P(),
            P(),
        ),
        out_specs=(P("scene", "seq", None), P("scene", "seq", None), P("scene", "seq", None), P()),
        check_vma=False,
    )
```

```python
import jax
import jax.numpy as jnp
from jax import lax
from jax.sharding import PartitionSpec as P


def on_device(
    scene_x, cotangent, gate_gain, kernel, block_mix, across_mix, across_unmix, block_unmix
):
    f32 = jnp.float32
    bf16 = jnp.bfloat16
    scenes_here, row_count, channels = scene_x.shape
    block_len = block_mix.shape[0]
    local_a = row_count // block_len
    parts = lax.axis_size("seq")
    chunk = block_len // parts
    kernel_f = kernel.astype(f32)

    inputs = scene_x.reshape(scenes_here, local_a, block_len, channels)
    upstream = cotangent.reshape(scenes_here, local_a, block_len, channels).astype(f32)
    gate_pre = inputs.astype(f32) * gate_gain
    gate_sig = jax.nn.sigmoid(gate_pre)
    gate = gate_pre * gate_sig
    grad_values = (upstream * gate).astype(bf16)
    mix_by_dest = block_mix.reshape(parts, chunk, block_len)
    unmix_by_dest = block_unmix.reshape(block_len, parts, chunk)
    first_mix = jnp.einsum(
        "Jjb,sabc->Jsajc", mix_by_dest, inputs, preferred_element_type=f32
    ).astype(bf16)
    grad_unmixed = jnp.einsum(
        "qJj,saqc->Jsajc", unmix_by_dest, grad_values, preferred_element_type=f32
    ).astype(bf16)
    outgoing = jnp.stack([first_mix, grad_unmixed], axis=1)
    incoming = lax.all_to_all(outgoing, "seq", split_axis=0, concat_axis=0, tiled=True)
    incoming = jnp.moveaxis(incoming, 2, 1)
    spread_mix = incoming[:, :, 0].reshape(parts, scenes_here, local_a, chunk, channels)
    spread_grad = incoming[:, :, 1].reshape(parts, scenes_here, local_a, chunk, channels)
    spread_mix = jnp.moveaxis(spread_mix, 1, 0).reshape(scenes_here, parts * local_a, chunk, channels)
    spread_grad = jnp.moveaxis(spread_grad, 1, 0).reshape(
        scenes_here, parts * local_a, chunk, channels
    )

    second_mix = jnp.einsum(
        "ia,sajc->sijc", across_mix, spread_mix, preferred_element_type=f32
    ).astype(bf16)
    weighted = (second_mix.astype(f32) * kernel_f).astype(bf16)
    unmixed = jnp.einsum(
        "pi,sijc->spjc", across_unmix, weighted, preferred_element_type=f32
    ).astype(bf16)
    grad_weighted = jnp.einsum(
        "pi,spjc->sijc", across_unmix, spread_grad, preferred_element_type=f32
    )
    kernel_term = jnp.sum(grad_weighted * second_mix.astype(f32), axis=0)
    scene_parts = lax.axis_size("scene")
    term_by_dest = kernel_term.reshape(scene_parts, block_len // scene_parts, chunk, channels)
    term_spread = lax.all_to_all(
        term_by_dest.astype(bf16), "scene", split_axis=0, concat_axis=0, tiled=True
    )
    kernel_grad = jnp.sum(term_spread.astype(f32), axis=0)
    grad_second = (grad_weighted * kernel_f).astype(bf16)
    grad_first = jnp.einsum(
        "ia,sijc->sajc", across_mix, grad_second, preferred_element_type=f32
    ).astype(bf16)
    back = jnp.stack(
        [
            unmixed.reshape(scenes_here, parts, local_a, chunk, channels),
            grad_first.reshape(scenes_here, parts, local_a, chunk, channels),
        ],
        axis=2,
    )
    back = jnp.moveaxis(back, 1, 0)
    returned = lax.all_to_all(back, "seq", split_axis=0, concat_axis=0, tiled=True)
    values = jnp.einsum(
        "qJj,Jsajc->saqc",
        unmix_by_dest,
        returned[:, :, 0],
        preferred_element_type=f32,
    )
    mixed_out = (values * gate).astype(bf16).reshape(scenes_here, row_count, channels)
    grad_gate = upstream * values * gate_sig * (1.0 + gate_pre * (1.0 - gate_sig))
    grad_input = (
        jnp.einsum("Jjb,Jsajc->sabc", mix_by_dest, returned[:, :, 1], preferred_element_type=f32)
        + grad_gate * gate_gain
    )
    grad_input = grad_input.astype(bf16).reshape(scenes_here, row_count, channels)
    gain_term = jnp.sum(inputs.astype(f32) * grad_gate, axis=(0, 1, 2))
    devices = lax.axis_size(("scene", "seq"))
    gain_spread = lax.all_to_all(
        jnp.broadcast_to(gain_term, (devices, channels)),
        ("scene", "seq"),
        split_axis=0,
        concat_axis=0,
        tiled=True,
    )
    gain_total = jnp.sum(gain_spread, axis=0)
    total_rows = scenes_here * lax.axis_size("scene") * local_a * parts * block_len
    grad_scale = 1.0 / jnp.sqrt(jnp.float32(total_rows))
    return (mixed_out, grad_input, kernel_grad, gain_total * grad_scale)


def solution(mesh):
    return jax.shard_map(
        on_device,
        mesh=mesh,
        in_specs=(
            P("scene", "seq", None),
            P("scene", "seq", None),
            P(),
            P(None, "seq", None),
            P(),
            P(),
            P(),
            P(),
        ),
        out_specs=(P("scene", "seq", None), P("scene", "seq", None), P("scene", "seq", None), P()),
        check_vma=False,
    )
```

```python
import jax
import jax.numpy as jnp
from jax import lax
from jax.sharding import PartitionSpec as P


def on_device(
    scene_x, cotangent, gate_gain, kernel, block_mix, across_mix, across_unmix, block_unmix
):
    f32 = jnp.float32
    bf16 = jnp.bfloat16
    scenes_here, row_count, channels = scene_x.shape
    block_len = block_mix.shape[0]
    local_a = row_count // block_len
    parts = lax.axis_size("seq")
    chunk = block_len // parts
    kernel_f = kernel.astype(f32)

    inputs = scene_x.reshape(scenes_here, local_a, block_len, channels)
    upstream = cotangent.reshape(scenes_here, local_a, block_len, channels).astype(f32)
    gate_pre = inputs.astype(f32) * gate_gain
    gate_sig = jax.nn.sigmoid(gate_pre)
    gate = gate_pre * gate_sig
    grad_values = (upstream * gate).astype(bf16)
    mix_by_dest = block_mix.reshape(parts, chunk, block_len)
    unmix_by_dest = block_unmix.reshape(block_len, parts, chunk)
    first_mix = jnp.einsum(
        "Jjb,sabc->Jsajc", mix_by_dest, inputs, preferred_element_type=f32
    ).astype(bf16)
    grad_unmixed = jnp.einsum(
        "qJj,saqc->Jsajc", unmix_by_dest, grad_values, preferred_element_type=f32
    ).astype(bf16)
    outgoing = jnp.stack([first_mix, grad_unmixed], axis=1)
    incoming = lax.all_to_all(outgoing, "seq", split_axis=0, concat_axis=0, tiled=True)
    incoming = jnp.moveaxis(incoming, 2, 1)
    spread_mix = incoming[:, :, 0].reshape(parts, scenes_here, local_a, chunk, channels)
    spread_grad = incoming[:, :, 1].reshape(parts, scenes_here, local_a, chunk, channels)
    spread_mix = jnp.moveaxis(spread_mix, 1, 0).reshape(scenes_here, parts * local_a, chunk, channels)
    spread_grad = jnp.moveaxis(spread_grad, 1, 0).reshape(
        scenes_here, parts * local_a, chunk, channels
    )

    second_mix = jnp.einsum(
        "ia,sajc->sijc", across_mix, spread_mix, preferred_element_type=f32
    ).astype(bf16)
    weighted = (second_mix.astype(f32) * kernel_f).astype(bf16)
    unmixed = jnp.einsum(
        "pi,sijc->spjc", across_unmix, weighted, preferred_element_type=f32
    ).astype(bf16)
    grad_weighted = jnp.einsum(
        "pi,spjc->sijc", across_unmix, spread_grad, preferred_element_type=f32
    )
    kernel_term = jnp.sum(grad_weighted * second_mix.astype(f32), axis=0)
    scene_parts = lax.axis_size("scene")
    term_by_dest = kernel_term.reshape(scene_parts, block_len // scene_parts, chunk, channels)
    term_by_dest = term_by_dest.astype(bf16)
    scene_index = lax.axis_index("scene")
    kernel_grad = lax.dynamic_index_in_dim(term_by_dest, scene_index, 0, False).astype(f32)
    for shift in range(1, scene_parts):
        outgoing_term = lax.dynamic_index_in_dim(
            term_by_dest, (scene_index + shift) % scene_parts, 0, False
        )
        pairs = [(src, (src + shift) % scene_parts) for src in range(scene_parts)]
        kernel_grad = kernel_grad + lax.ppermute(outgoing_term, "scene", pairs).astype(f32)
    grad_second = (grad_weighted * kernel_f).astype(bf16)
    grad_first = jnp.einsum(
        "ia,sijc->sajc", across_mix, grad_second, preferred_element_type=f32
    ).astype(bf16)
    back = jnp.stack(
        [
            unmixed.reshape(scenes_here, parts, local_a, chunk, channels),
            grad_first.reshape(scenes_here, parts, local_a, chunk, channels),
        ],
        axis=2,
    )
    back = jnp.moveaxis(back, 1, 0)
    returned = lax.all_to_all(back, "seq", split_axis=0, concat_axis=0, tiled=True)
    values = jnp.einsum(
        "qJj,Jsajc->saqc",
        unmix_by_dest,
        returned[:, :, 0],
        preferred_element_type=f32,
    )
    mixed_out = (values * gate).astype(bf16).reshape(scenes_here, row_count, channels)
    grad_gate = upstream * values * gate_sig * (1.0 + gate_pre * (1.0 - gate_sig))
    grad_input = (
        jnp.einsum("Jjb,Jsajc->sabc", mix_by_dest, returned[:, :, 1], preferred_element_type=f32)
        + grad_gate * gate_gain
    )
    grad_input = grad_input.astype(bf16).reshape(scenes_here, row_count, channels)
    gain_term = jnp.sum(inputs.astype(f32) * grad_gate, axis=(0, 1, 2))
    devices = lax.axis_size(("scene", "seq"))
    gain_spread = lax.all_to_all(
        jnp.broadcast_to(gain_term, (devices, channels)),
        ("scene", "seq"),
        split_axis=0,
        concat_axis=0,
        tiled=True,
    )
    gain_total = jnp.sum(gain_spread, axis=0)
    total_rows = scenes_here * lax.axis_size("scene") * local_a * parts * block_len
    grad_scale = 1.0 / jnp.sqrt(jnp.float32(total_rows))
    return (mixed_out, grad_input, kernel_grad, gain_total * grad_scale)


def solution(mesh):
    return jax.shard_map(
        on_device,
        mesh=mesh,
        in_specs=(
            P("scene", "seq", None),
            P("scene", "seq", None),
            P(),
            P(None, "seq", None),
            P(),
            P(),
            P(),
            P(),
        ),
        out_specs=(P("scene", "seq", None), P("scene", "seq", None), P("scene", "seq", None), P()),
        check_vma=False,
    )
```

```python
import jax
import jax.numpy as jnp
from jax import lax
from jax.sharding import PartitionSpec as P


def on_device(
    scene_x, cotangent, gate_gain, kernel, block_mix, across_mix, across_unmix, block_unmix
):
    f32 = jnp.float32
    bf16 = jnp.bfloat16
    scenes_here, row_count, channels = scene_x.shape
    block_len = block_mix.shape[0]
    local_a = row_count // block_len
    parts = lax.axis_size("seq")
    chunk = block_len // parts
    kernel_f = kernel.astype(f32)

    inputs = scene_x.reshape(scenes_here, local_a, block_len, channels)
    upstream = cotangent.reshape(scenes_here, local_a, block_len, channels).astype(f32)
    gate_pre = inputs.astype(f32) * gate_gain
    gate_sig = jax.nn.sigmoid(gate_pre)
    gate = gate_pre * gate_sig
    grad_values = (upstream * gate).astype(bf16)
    mix_by_dest = block_mix.reshape(parts, chunk, block_len)
    unmix_by_dest = block_unmix.reshape(block_len, parts, chunk)
    first_mix = jnp.einsum(
        "Jjb,sabc->Jsajc", mix_by_dest, inputs, preferred_element_type=f32
    ).astype(bf16)
    grad_unmixed = jnp.einsum(
        "qJj,saqc->Jsajc", unmix_by_dest, grad_values, preferred_element_type=f32
    ).astype(bf16)
    outgoing = jnp.stack([first_mix, grad_unmixed], axis=1)
    incoming = lax.all_to_all(outgoing, "seq", split_axis=0, concat_axis=0, tiled=True)
    incoming = jnp.moveaxis(incoming, 2, 1)
    spread_mix = incoming[:, :, 0].reshape(parts, scenes_here, local_a, chunk, channels)
    spread_grad = incoming[:, :, 1].reshape(parts, scenes_here, local_a, chunk, channels)
    spread_mix = jnp.moveaxis(spread_mix, 1, 0).reshape(scenes_here, parts * local_a, chunk, channels)
    spread_grad = jnp.moveaxis(spread_grad, 1, 0).reshape(
        scenes_here, parts * local_a, chunk, channels
    )

    second_mix = jnp.einsum(
        "ia,sajc->sijc", across_mix, spread_mix, preferred_element_type=f32
    ).astype(bf16)
    weighted = (second_mix.astype(f32) * kernel_f).astype(bf16)
    unmixed = jnp.einsum(
        "pi,sijc->spjc", across_unmix, weighted, preferred_element_type=f32
    ).astype(bf16)
    grad_weighted = jnp.einsum(
        "pi,spjc->sijc", across_unmix, spread_grad, preferred_element_type=f32
    )
    kernel_term = jnp.sum(grad_weighted * second_mix.astype(f32), axis=0)
    scene_parts = lax.axis_size("scene")
    inner = 4 if scene_parts % 4 == 0 else 1
    outer = scene_parts // inner
    scene_index = lax.axis_index("scene")
    outer_index = scene_index // inner
    inner_index = scene_index % inner
    term_by_dest = kernel_term.reshape(outer, inner, block_len // scene_parts, chunk, channels)
    term_sent = term_by_dest.astype(bf16)
    partial = lax.dynamic_index_in_dim(term_by_dest, outer_index, 0, False)
    for shift in range(1, outer):
        piece = lax.dynamic_index_in_dim(term_sent, (outer_index + shift) % outer, 0, False)
        pairs = [
            (o * inner + k, ((o + shift) % outer) * inner + k)
            for o in range(outer)
            for k in range(inner)
        ]
        partial = partial + lax.ppermute(piece, "scene", pairs).astype(f32)
    kernel_grad = lax.dynamic_index_in_dim(partial, inner_index, 0, False)
    for shift in range(1, inner):
        piece = lax.dynamic_index_in_dim(partial, (inner_index + shift) % inner, 0, False)
        pairs = [
            (o * inner + k, o * inner + (k + shift) % inner)
            for o in range(outer)
            for k in range(inner)
        ]
        kernel_grad = kernel_grad + lax.ppermute(piece, "scene", pairs)
    grad_second = (grad_weighted * kernel_f).astype(bf16)
    grad_first = jnp.einsum(
        "ia,sijc->sajc", across_mix, grad_second, preferred_element_type=f32
    ).astype(bf16)
    back = jnp.stack(
        [
            unmixed.reshape(scenes_here, parts, local_a, chunk, channels),
            grad_first.reshape(scenes_here, parts, local_a, chunk, channels),
        ],
        axis=2,
    )
    back = jnp.moveaxis(back, 1, 0)
    returned = lax.all_to_all(back, "seq", split_axis=0, concat_axis=0, tiled=True)
    values = jnp.einsum(
        "qJj,Jsajc->saqc",
        unmix_by_dest,
        returned[:, :, 0],
        preferred_element_type=f32,
    )
    mixed_out = (values * gate).astype(bf16).reshape(scenes_here, row_count, channels)
    grad_gate = upstream * values * gate_sig * (1.0 + gate_pre * (1.0 - gate_sig))
    grad_input = (
        jnp.einsum("Jjb,Jsajc->sabc", mix_by_dest, returned[:, :, 1], preferred_element_type=f32)
        + grad_gate * gate_gain
    )
    grad_input = grad_input.astype(bf16).reshape(scenes_here, row_count, channels)
    gain_term = jnp.sum(inputs.astype(f32) * grad_gate, axis=(0, 1, 2))
    devices = lax.axis_size(("scene", "seq"))
    gain_spread = lax.all_to_all(
        jnp.broadcast_to(gain_term, (devices, channels)),
        ("scene", "seq"),
        split_axis=0,
        concat_axis=0,
        tiled=True,
    )
    gain_total = jnp.sum(gain_spread, axis=0)
    total_rows = scenes_here * lax.axis_size("scene") * local_a * parts * block_len
    grad_scale = 1.0 / jnp.sqrt(jnp.float32(total_rows))
    return (mixed_out, grad_input, kernel_grad, gain_total * grad_scale)


def solution(mesh):
    return jax.shard_map(
        on_device,
        mesh=mesh,
        in_specs=(
            P("scene", "seq", None),
            P("scene", "seq", None),
            P(),
            P(None, "seq", None),
            P(),
            P(),
            P(),
            P(),
        ),
        out_specs=(P("scene", "seq", None), P("scene", "seq", None), P("scene", "seq", None), P()),
        check_vma=False,
    )
```

```python
import jax
import jax.numpy as jnp
from jax import lax
from jax.sharding import PartitionSpec as P


def on_device(
    scene_x, cotangent, gate_gain, kernel, block_mix, across_mix, across_unmix, block_unmix
):
    f32 = jnp.float32
    bf16 = jnp.bfloat16
    scenes_here, row_count, channels = scene_x.shape
    block_len = block_mix.shape[0]
    local_a = row_count // block_len
    parts = lax.axis_size("seq")
    chunk = block_len // parts
    kernel_f = kernel.astype(f32)

    inputs = scene_x.reshape(scenes_here, local_a, block_len, channels)
    upstream = cotangent.reshape(scenes_here, local_a, block_len, channels).astype(f32)
    gate_pre = inputs.astype(f32) * gate_gain
    gate_sig = jax.nn.sigmoid(gate_pre)
    gate = gate_pre * gate_sig
    grad_values = (upstream * gate).astype(bf16)
    mix_by_dest = block_mix.reshape(parts, chunk, block_len)
    unmix_by_dest = block_unmix.reshape(block_len, parts, chunk)
    first_mix = jnp.einsum(
        "Jjb,sabc->Jsajc", mix_by_dest, inputs, preferred_element_type=f32
    ).astype(bf16)
    grad_unmixed = jnp.einsum(
        "qJj,saqc->Jsajc", unmix_by_dest, grad_values, preferred_element_type=f32
    ).astype(bf16)
    outgoing = jnp.stack([first_mix, grad_unmixed], axis=1)
    incoming = lax.all_to_all(outgoing, "seq", split_axis=0, concat_axis=0, tiled=True)
    incoming = jnp.moveaxis(incoming, 2, 1)
    spread_mix = incoming[:, :, 0].reshape(parts, scenes_here, local_a, chunk, channels)
    spread_grad = incoming[:, :, 1].reshape(parts, scenes_here, local_a, chunk, channels)
    spread_mix = jnp.moveaxis(spread_mix, 1, 0).reshape(scenes_here, parts * local_a, chunk, channels)
    spread_grad = jnp.moveaxis(spread_grad, 1, 0).reshape(
        scenes_here, parts * local_a, chunk, channels
    )

    second_mix = jnp.einsum(
        "ia,sajc->sijc", across_mix, spread_mix, preferred_element_type=f32
    ).astype(bf16)
    weighted = (second_mix.astype(f32) * kernel_f).astype(bf16)
    unmixed = jnp.einsum(
        "pi,sijc->spjc", across_unmix, weighted, preferred_element_type=f32
    ).astype(bf16)
    grad_weighted = jnp.einsum(
        "pi,spjc->sijc", across_unmix, spread_grad, preferred_element_type=f32
    )
    kernel_term = jnp.sum(grad_weighted * second_mix.astype(f32), axis=0)
    scene_parts = lax.axis_size("scene")
    inner = 4 if scene_parts % 4 == 0 else 1
    outer = scene_parts // inner
    scene_index = lax.axis_index("scene")
    outer_index = scene_index // inner
    inner_index = scene_index % inner
    term_by_dest = kernel_term.reshape(outer, inner, block_len // scene_parts, chunk, channels)
    term_sent = term_by_dest.astype(bf16)
    partial = lax.dynamic_index_in_dim(term_by_dest, outer_index, 0, False)
    for shift in range(1, outer):
        piece = lax.dynamic_index_in_dim(term_sent, (outer_index + shift) % outer, 0, False)
        pairs = [
            (o * inner + k, ((o + shift) % outer) * inner + k)
            for o in range(outer)
            for k in range(inner)
        ]
        partial = partial + lax.ppermute(piece, "scene", pairs).astype(f32)
    kernel_grad = lax.dynamic_index_in_dim(partial, inner_index, 0, False)
    partial_sent = partial.astype(bf16)
    for shift in range(1, inner):
        piece = lax.dynamic_index_in_dim(partial_sent, (inner_index + shift) % inner, 0, False)
        pairs = [
            (o * inner + k, o * inner + (k + shift) % inner)
            for o in range(outer)
            for k in range(inner)
        ]
        kernel_grad = kernel_grad + lax.ppermute(piece, "scene", pairs).astype(f32)
    grad_second = (grad_weighted * kernel_f).astype(bf16)
    grad_first = jnp.einsum(
        "ia,sijc->sajc", across_mix, grad_second, preferred_element_type=f32
    ).astype(bf16)
    back = jnp.stack(
        [
            unmixed.reshape(scenes_here, parts, local_a, chunk, channels),
            grad_first.reshape(scenes_here, parts, local_a, chunk, channels),
        ],
        axis=2,
    )
    back = jnp.moveaxis(back, 1, 0)
    returned = lax.all_to_all(back, "seq", split_axis=0, concat_axis=0, tiled=True)
    values = jnp.einsum(
        "qJj,Jsajc->saqc",
        unmix_by_dest,
        returned[:, :, 0],
        preferred_element_type=f32,
    )
    mixed_out = (values * gate).astype(bf16).reshape(scenes_here, row_count, channels)
    grad_gate = upstream * values * gate_sig * (1.0 + gate_pre * (1.0 - gate_sig))
    grad_input = (
        jnp.einsum("Jjb,Jsajc->sabc", mix_by_dest, returned[:, :, 1], preferred_element_type=f32)
        + grad_gate * gate_gain
    )
    grad_input = grad_input.astype(bf16).reshape(scenes_here, row_count, channels)
    gain_term = jnp.sum(inputs.astype(f32) * grad_gate, axis=(0, 1, 2))
    devices = lax.axis_size(("scene", "seq"))
    gain_spread = lax.all_to_all(
        jnp.broadcast_to(gain_term, (devices, channels)),
        ("scene", "seq"),
        split_axis=0,
        concat_axis=0,
        tiled=True,
    )
    gain_total = jnp.sum(gain_spread, axis=0)
    total_rows = scenes_here * lax.axis_size("scene") * local_a * parts * block_len
    grad_scale = 1.0 / jnp.sqrt(jnp.float32(total_rows))
    return (mixed_out, grad_input, kernel_grad, gain_total * grad_scale)


def solution(mesh):
    return jax.shard_map(
        on_device,
        mesh=mesh,
        in_specs=(
            P("scene", "seq", None),
            P("scene", "seq", None),
            P(),
            P(None, "seq", None),
            P(),
            P(),
            P(),
            P(),
        ),
        out_specs=(P("scene", "seq", None), P("scene", "seq", None), P("scene", "seq", None), P()),
        check_vma=False,
    )
```

```python
import jax
import jax.numpy as jnp
from jax import lax
from jax.sharding import PartitionSpec as P

CHANNEL_GROUPS = 2


def on_device(
    scene_x, cotangent, gate_gain, kernel, block_mix, across_mix, across_unmix, block_unmix
):
    f32 = jnp.float32
    bf16 = jnp.bfloat16
    scenes_here, row_count, channels = scene_x.shape
    block_len = block_mix.shape[0]
    local_a = row_count // block_len
    parts = lax.axis_size("seq")
    chunk = block_len // parts
    width = channels // CHANNEL_GROUPS
    mix_by_dest = block_mix.reshape(parts, chunk, block_len)
    unmix_by_dest = block_unmix.reshape(block_len, parts, chunk)

    def first_phase(g):
        cols = slice(g * width, (g + 1) * width)
        inputs = scene_x[:, :, cols].reshape(scenes_here, local_a, block_len, width)
        upstream = cotangent[:, :, cols].reshape(scenes_here, local_a, block_len, width)
        gain_g = gate_gain[cols]
        gate_pre = inputs.astype(f32) * gain_g
        gate_sig = jax.nn.sigmoid(gate_pre)
        grad_values = (upstream.astype(f32) * gate_pre * gate_sig).astype(bf16)
        first_mix = jnp.einsum(
            "Jjb,sabc->Jsajc", mix_by_dest, inputs, preferred_element_type=f32
        ).astype(bf16)
        grad_unmixed = jnp.einsum(
            "qJj,saqc->Jsajc", unmix_by_dest, grad_values, preferred_element_type=f32
        ).astype(bf16)
        return jnp.stack([first_mix, grad_unmixed], axis=1)

    def middle_phase(g, incoming):
        cols = slice(g * width, (g + 1) * width)
        kernel_f = kernel[:, :, cols].astype(f32)
        incoming = jnp.moveaxis(incoming, 2, 1)
        spread_mix = incoming[:, :, 0]
        spread_grad = incoming[:, :, 1]
        spread_mix = jnp.moveaxis(spread_mix, 1, 0).reshape(
            scenes_here, parts * local_a, chunk, width
        )
        spread_grad = jnp.moveaxis(spread_grad, 1, 0).reshape(
            scenes_here, parts * local_a, chunk, width
        )
        second_mix = jnp.einsum(
            "ia,sajc->sijc", across_mix, spread_mix, preferred_element_type=f32
        ).astype(bf16)
        weighted = (second_mix.astype(f32) * kernel_f).astype(bf16)
        unmixed = jnp.einsum(
            "pi,sijc->spjc", across_unmix, weighted, preferred_element_type=f32
        ).astype(bf16)
        grad_weighted = jnp.einsum(
            "pi,spjc->sijc", across_unmix, spread_grad, preferred_element_type=f32
        )
        kernel_term = jnp.sum(grad_weighted * second_mix.astype(f32), axis=0)
        grad_second = (grad_weighted * kernel_f).astype(bf16)
        grad_first = jnp.einsum(
            "ia,sijc->sajc", across_mix, grad_second, preferred_element_type=f32
        ).astype(bf16)
        back = jnp.stack(
            [
                unmixed.reshape(scenes_here, parts, local_a, chunk, width),
                grad_first.reshape(scenes_here, parts, local_a, chunk, width),
            ],
            axis=2,
        )
        return jnp.moveaxis(back, 1, 0), kernel_term

    def last_phase(g, returned):
        cols = slice(g * width, (g + 1) * width)
        inputs = scene_x[:, :, cols].reshape(scenes_here, local_a, block_len, width).astype(f32)
        upstream = cotangent[:, :, cols].reshape(scenes_here, local_a, block_len, width)
        upstream = upstream.astype(f32)
        gain_g = gate_gain[cols]
        gate_pre = inputs * gain_g
        gate_sig = jax.nn.sigmoid(gate_pre)
        values = jnp.einsum(
            "qJj,Jsajc->saqc", unmix_by_dest, returned[:, :, 0], preferred_element_type=f32
        )
        mixed_out = (values * gate_pre * gate_sig).astype(bf16)
        grad_gate = upstream * values * gate_sig * (1.0 + gate_pre * (1.0 - gate_sig))
        grad_input = (
            jnp.einsum(
                "Jjb,Jsajc->sabc", mix_by_dest, returned[:, :, 1], preferred_element_type=f32
            )
            + grad_gate * gain_g
        ).astype(bf16)
        gain_term = jnp.sum(inputs * grad_gate, axis=(0, 1, 2))
        return mixed_out, grad_input, gain_term

    outgoing = [first_phase(g) for g in range(CHANNEL_GROUPS)]
    incoming = [
        lax.all_to_all(o, "seq", split_axis=0, concat_axis=0, tiled=True) for o in outgoing
    ]
    middles = [middle_phase(g, incoming[g]) for g in range(CHANNEL_GROUPS)]
    returned = [
        lax.all_to_all(m[0], "seq", split_axis=0, concat_axis=0, tiled=True) for m in middles
    ]
    lasts = [last_phase(g, returned[g]) for g in range(CHANNEL_GROUPS)]
    mixed_out = jnp.concatenate([l[0] for l in lasts], axis=-1)
    grad_input = jnp.concatenate([l[1] for l in lasts], axis=-1)
    mixed_out = mixed_out.reshape(scenes_here, row_count, channels)
    grad_input = grad_input.reshape(scenes_here, row_count, channels)
    gain_term = jnp.concatenate([l[2] for l in lasts], axis=-1)
    kernel_term = jnp.concatenate([m[1] for m in middles], axis=-1)

    scene_parts = lax.axis_size("scene")
    inner = 4 if scene_parts % 4 == 0 else 1
    outer = scene_parts // inner
    scene_index = lax.axis_index("scene")
    outer_index = scene_index // inner
    inner_index = scene_index % inner
    term_by_dest = kernel_term.reshape(outer, inner, block_len // scene_parts, chunk, channels)
    term_sent = term_by_dest.astype(bf16)
    partial = lax.dynamic_index_in_dim(term_by_dest, outer_index, 0, False)
    for shift in range(1, outer):
        piece = lax.dynamic_index_in_dim(term_sent, (outer_index + shift) % outer, 0, False)
        pairs = [
            (o * inner + k, ((o + shift) % outer) * inner + k)
            for o in range(outer)
            for k in range(inner)
        ]
        partial = partial + lax.ppermute(piece, "scene", pairs).astype(f32)
    kernel_grad = lax.dynamic_index_in_dim(partial, inner_index, 0, False)
    partial_sent = partial.astype(bf16)
    for shift in range(1, inner):
        piece = lax.dynamic_index_in_dim(partial_sent, (inner_index + shift) % inner, 0, False)
        pairs = [
            (o * inner + k, o * inner + (k + shift) % inner)
            for o in range(outer)
            for k in range(inner)
        ]
        kernel_grad = kernel_grad + lax.ppermute(piece, "scene", pairs).astype(f32)

    devices = lax.axis_size(("scene", "seq"))
    gain_spread = lax.all_to_all(
        jnp.broadcast_to(gain_term, (devices, channels)),
        ("scene", "seq"),
        split_axis=0,
        concat_axis=0,
        tiled=True,
    )
    gain_total = jnp.sum(gain_spread, axis=0)
    total_rows = scenes_here * scene_parts * local_a * parts * block_len
    grad_scale = 1.0 / jnp.sqrt(jnp.float32(total_rows))
    return (mixed_out, grad_input, kernel_grad, gain_total * grad_scale)


def solution(mesh):
    return jax.shard_map(
        on_device,
        mesh=mesh,
        in_specs=(
            P("scene", "seq", None),
            P("scene", "seq", None),
            P(),
            P(None, "seq", None),
            P(),
            P(),
            P(),
            P(),
        ),
        out_specs=(P("scene", "seq", None), P("scene", "seq", None), P("scene", "seq", None), P()),
        check_vma=False,
    )
```

```python
import jax
import jax.numpy as jnp
from jax import lax
from jax.sharding import PartitionSpec as P


def on_device(
    scene_x, cotangent, gate_gain, kernel, block_mix, across_mix, across_unmix, block_unmix
):
    f32 = jnp.float32
    bf16 = jnp.bfloat16
    scenes_here, row_count, channels = scene_x.shape
    block_len = block_mix.shape[0]
    local_a = row_count // block_len
    parts = lax.axis_size("seq")
    chunk = block_len // parts
    kernel_f = kernel.astype(f32)

    inputs = scene_x.reshape(scenes_here, local_a, block_len, channels)
    upstream = cotangent.reshape(scenes_here, local_a, block_len, channels).astype(f32)
    gate_pre = inputs.astype(f32) * gate_gain
    gate_sig = jax.nn.sigmoid(gate_pre)
    gate = gate_pre * gate_sig
    grad_values = (upstream * gate).astype(bf16)
    mix_by_dest = block_mix.reshape(parts, chunk, block_len)
    unmix_by_dest = block_unmix.reshape(block_len, parts, chunk)
    first_mix = jnp.einsum(
        "Jjb,sabc->Jsajc", mix_by_dest, inputs, preferred_element_type=f32
    ).astype(bf16)
    grad_unmixed = jnp.einsum(
        "qJj,saqc->Jsajc", unmix_by_dest, grad_values, preferred_element_type=f32
    ).astype(bf16)
    gate_weight = (
        inputs.astype(f32) * upstream * gate_sig * (1.0 + gate_pre * (1.0 - gate_sig))
    )
    weight_hi = gate_weight.astype(bf16)
    weight_lo = (gate_weight - weight_hi.astype(f32)).astype(bf16)
    gain_weight = jnp.einsum(
        "qJj,saqc->Jsajc", unmix_by_dest, weight_hi, preferred_element_type=f32
    ) + jnp.einsum("qJj,saqc->Jsajc", unmix_by_dest, weight_lo, preferred_element_type=f32)
    outgoing = jnp.stack([first_mix, grad_unmixed], axis=1)
    incoming = lax.all_to_all(outgoing, "seq", split_axis=0, concat_axis=0, tiled=True)
    incoming = jnp.moveaxis(incoming, 2, 1)
    spread_mix = incoming[:, :, 0].reshape(parts, scenes_here, local_a, chunk, channels)
    spread_grad = incoming[:, :, 1].reshape(parts, scenes_here, local_a, chunk, channels)
    spread_mix = jnp.moveaxis(spread_mix, 1, 0).reshape(scenes_here, parts * local_a, chunk, channels)
    spread_grad = jnp.moveaxis(spread_grad, 1, 0).reshape(
        scenes_here, parts * local_a, chunk, channels
    )

    second_mix = jnp.einsum(
        "ia,sajc->sijc", across_mix, spread_mix, preferred_element_type=f32
    ).astype(bf16)
    weighted = (second_mix.astype(f32) * kernel_f).astype(bf16)
    unmixed = jnp.einsum(
        "pi,sijc->spjc", across_unmix, weighted, preferred_element_type=f32
    ).astype(bf16)
    grad_weighted = jnp.einsum(
        "pi,spjc->sijc", across_unmix, spread_grad, preferred_element_type=f32
    )
    kernel_term = jnp.sum(grad_weighted * second_mix.astype(f32), axis=0)
    scene_parts = lax.axis_size("scene")
    inner = 4 if scene_parts % 4 == 0 else 1
    outer = scene_parts // inner
    scene_index = lax.axis_index("scene")
    outer_index = scene_index // inner
    inner_index = scene_index % inner
    term_by_dest = kernel_term.reshape(outer, inner, block_len // scene_parts, chunk, channels)
    term_sent = term_by_dest.astype(bf16)
    partial = lax.dynamic_index_in_dim(term_by_dest, outer_index, 0, False)
    for shift in range(1, outer):
        piece = lax.dynamic_index_in_dim(term_sent, (outer_index + shift) % outer, 0, False)
        pairs = [
            (o * inner + k, ((o + shift) % outer) * inner + k)
            for o in range(outer)
            for k in range(inner)
        ]
        partial = partial + lax.ppermute(piece, "scene", pairs).astype(f32)
    kernel_grad = lax.dynamic_index_in_dim(partial, inner_index, 0, False)
    partial_sent = partial.astype(bf16)
    for shift in range(1, inner):
        piece = lax.dynamic_index_in_dim(partial_sent, (inner_index + shift) % inner, 0, False)
        pairs = [
            (o * inner + k, o * inner + (k + shift) % inner)
            for o in range(outer)
            for k in range(inner)
        ]
        kernel_grad = kernel_grad + lax.ppermute(piece, "scene", pairs).astype(f32)
    grad_second = (grad_weighted * kernel_f).astype(bf16)
    grad_first = jnp.einsum(
        "ia,sijc->sajc", across_mix, grad_second, preferred_element_type=f32
    ).astype(bf16)
    back = jnp.stack(
        [
            unmixed.reshape(scenes_here, parts, local_a, chunk, channels),
            grad_first.reshape(scenes_here, parts, local_a, chunk, channels),
        ],
        axis=2,
    )
    back = jnp.moveaxis(back, 1, 0)
    returned = lax.all_to_all(back, "seq", split_axis=0, concat_axis=0, tiled=True)
    values = jnp.einsum(
        "qJj,Jsajc->saqc",
        unmix_by_dest,
        returned[:, :, 0],
        preferred_element_type=f32,
    )
    mixed_out = (values * gate).astype(bf16).reshape(scenes_here, row_count, channels)
    grad_gate = upstream * values * gate_sig * (1.0 + gate_pre * (1.0 - gate_sig))
    grad_input = (
        jnp.einsum("Jjb,Jsajc->sabc", mix_by_dest, returned[:, :, 1], preferred_element_type=f32)
        + grad_gate * gate_gain
    )
    grad_input = grad_input.astype(bf16).reshape(scenes_here, row_count, channels)
    gain_term = jnp.sum(returned[:, :, 0].astype(f32) * gain_weight, axis=(0, 1, 2, 3))
    devices = lax.axis_size(("scene", "seq"))
    gain_spread = lax.all_to_all(
        jnp.broadcast_to(gain_term, (devices, channels)),
        ("scene", "seq"),
        split_axis=0,
        concat_axis=0,
        tiled=True,
    )
    gain_total = jnp.sum(gain_spread, axis=0)
    total_rows = scenes_here * lax.axis_size("scene") * local_a * parts * block_len
    grad_scale = 1.0 / jnp.sqrt(jnp.float32(total_rows))
    return (mixed_out, grad_input, kernel_grad, gain_total * grad_scale)


def solution(mesh):
    return jax.shard_map(
        on_device,
        mesh=mesh,
        in_specs=(
            P("scene", "seq", None),
            P("scene", "seq", None),
            P(),
            P(None, "seq", None),
            P(),
            P(),
            P(),
            P(),
        ),
        out_specs=(P("scene", "seq", None), P("scene", "seq", None), P("scene", "seq", None), P()),
        check_vma=False,
    )
```

```python
import jax
import jax.numpy as jnp
from jax import lax
from jax.sharding import PartitionSpec as P


def on_device(
    scene_x, cotangent, gate_gain, kernel, block_mix, across_mix, across_unmix, block_unmix
):
    f32 = jnp.float32
    bf16 = jnp.bfloat16
    scenes_here, row_count, channels = scene_x.shape
    block_len = block_mix.shape[0]
    local_a = row_count // block_len
    parts = lax.axis_size("seq")
    chunk = block_len // parts
    kernel_f = kernel.astype(f32)

    inputs = scene_x.reshape(scenes_here, local_a, block_len, channels)
    upstream = cotangent.reshape(scenes_here, local_a, block_len, channels).astype(f32)
    gate_pre = inputs.astype(f32) * gate_gain
    gate_sig = jax.nn.sigmoid(gate_pre)
    gate = gate_pre * gate_sig
    grad_values = (upstream * gate).astype(bf16)
    mix_by_dest = block_mix.reshape(parts, chunk, block_len)
    unmix_by_dest = block_unmix.reshape(block_len, parts, chunk)
    first_mix = jnp.einsum(
        "Jjb,sabc->Jsajc", mix_by_dest, inputs, preferred_element_type=f32
    ).astype(bf16)
    grad_unmixed = jnp.einsum(
        "qJj,saqc->Jsajc", unmix_by_dest, grad_values, preferred_element_type=f32
    ).astype(bf16)
    outgoing = jnp.stack([first_mix, grad_unmixed], axis=1)
    incoming = lax.all_to_all(outgoing, "seq", split_axis=0, concat_axis=0, tiled=True)
    incoming = jnp.moveaxis(incoming, 2, 1)
    spread_mix = incoming[:, :, 0].reshape(parts, scenes_here, local_a, chunk, channels)
    spread_grad = incoming[:, :, 1].reshape(parts, scenes_here, local_a, chunk, channels)
    spread_mix = jnp.moveaxis(spread_mix, 1, 0).reshape(scenes_here, parts * local_a, chunk, channels)
    spread_grad = jnp.moveaxis(spread_grad, 1, 0).reshape(
        scenes_here, parts * local_a, chunk, channels
    )

    flat = chunk * channels
    spread_mix = spread_mix.reshape(scenes_here, block_len, flat)
    spread_grad = spread_grad.reshape(scenes_here, block_len, flat)
    kernel_f = kernel_f.reshape(block_len, flat)
    second_mix = jnp.einsum(
        "ia,san->sin", across_mix, spread_mix, preferred_element_type=f32
    ).astype(bf16)
    weighted = (second_mix.astype(f32) * kernel_f).astype(bf16)
    unmixed = jnp.einsum(
        "pi,sin->spn", across_unmix, weighted, preferred_element_type=f32
    ).astype(bf16)
    grad_weighted = jnp.einsum(
        "pi,spn->sin", across_unmix, spread_grad, preferred_element_type=f32
    )
    kernel_term = jnp.sum(grad_weighted * second_mix.astype(f32), axis=0)
    scene_parts = lax.axis_size("scene")
    inner = 4 if scene_parts % 4 == 0 else 1
    outer = scene_parts // inner
    scene_index = lax.axis_index("scene")
    outer_index = scene_index // inner
    inner_index = scene_index % inner
    term_by_dest = kernel_term.reshape(outer, inner, block_len // scene_parts, chunk, channels)
    term_sent = term_by_dest.astype(bf16)
    partial = lax.dynamic_index_in_dim(term_by_dest, outer_index, 0, False)
    for shift in range(1, outer):
        piece = lax.dynamic_index_in_dim(term_sent, (outer_index + shift) % outer, 0, False)
        pairs = [
            (o * inner + k, ((o + shift) % outer) * inner + k)
            for o in range(outer)
            for k in range(inner)
        ]
        partial = partial + lax.ppermute(piece, "scene", pairs).astype(f32)
    kernel_grad = lax.dynamic_index_in_dim(partial, inner_index, 0, False)
    partial_sent = partial.astype(bf16)
    for shift in range(1, inner):
        piece = lax.dynamic_index_in_dim(partial_sent, (inner_index + shift) % inner, 0, False)
        pairs = [
            (o * inner + k, o * inner + (k + shift) % inner)
            for o in range(outer)
            for k in range(inner)
        ]
        kernel_grad = kernel_grad + lax.ppermute(piece, "scene", pairs).astype(f32)
    grad_second = (grad_weighted * kernel_f).astype(bf16)
    grad_first = jnp.einsum(
        "ia,sin->san", across_mix, grad_second, preferred_element_type=f32
    ).astype(bf16)
    back = jnp.stack(
        [
            unmixed.reshape(scenes_here, parts, local_a, chunk, channels),
            grad_first.reshape(scenes_here, parts, local_a, chunk, channels),
        ],
        axis=2,
    )
    back = jnp.moveaxis(back, 1, 0)
    returned = lax.all_to_all(back, "seq", split_axis=0, concat_axis=0, tiled=True)
    values = jnp.einsum(
        "qJj,Jsajc->saqc",
        unmix_by_dest,
        returned[:, :, 0],
        preferred_element_type=f32,
    )
    mixed_out = (values * gate).astype(bf16).reshape(scenes_here, row_count, channels)
    grad_gate = upstream * values * gate_sig * (1.0 + gate_pre * (1.0 - gate_sig))
    grad_input = (
        jnp.einsum("Jjb,Jsajc->sabc", mix_by_dest, returned[:, :, 1], preferred_element_type=f32)
        + grad_gate * gate_gain
    )
    grad_input = grad_input.astype(bf16).reshape(scenes_here, row_count, channels)
    gain_term = jnp.sum(inputs.astype(f32) * grad_gate, axis=(0, 1, 2))
    devices = lax.axis_size(("scene", "seq"))
    gain_spread = lax.all_to_all(
        jnp.broadcast_to(gain_term, (devices, channels)),
        ("scene", "seq"),
        split_axis=0,
        concat_axis=0,
        tiled=True,
    )
    gain_total = jnp.sum(gain_spread, axis=0)
    total_rows = scenes_here * lax.axis_size("scene") * local_a * parts * block_len
    grad_scale = 1.0 / jnp.sqrt(jnp.float32(total_rows))
    return (mixed_out, grad_input, kernel_grad, gain_total * grad_scale)


def solution(mesh):
    return jax.shard_map(
        on_device,
        mesh=mesh,
        in_specs=(
            P("scene", "seq", None),
            P("scene", "seq", None),
            P(),
            P(None, "seq", None),
            P(),
            P(),
            P(),
            P(),
        ),
        out_specs=(P("scene", "seq", None), P("scene", "seq", None), P("scene", "seq", None), P()),
        check_vma=False,
    )
```

```python
import jax
import jax.numpy as jnp
from jax import lax
from jax.sharding import PartitionSpec as P


def on_device(
    scene_x, cotangent, gate_gain, kernel, block_mix, across_mix, across_unmix, block_unmix
):
    f32 = jnp.float32
    bf16 = jnp.bfloat16
    scenes_here, row_count, channels = scene_x.shape
    block_len = block_mix.shape[0]
    local_a = row_count // block_len
    parts = lax.axis_size("seq")
    chunk = block_len // parts
    kernel_f = kernel.astype(f32)

    inputs = scene_x.reshape(scenes_here, local_a, block_len, channels)
    upstream = cotangent.reshape(scenes_here, local_a, block_len, channels).astype(f32)
    gate_pre = inputs.astype(f32) * gate_gain
    gate_sig = jax.nn.sigmoid(gate_pre)
    gate = gate_pre * gate_sig
    grad_values = (upstream * gate).astype(bf16)
    mix_by_dest = block_mix.reshape(parts, chunk, block_len)
    unmix_by_dest = block_unmix.reshape(block_len, parts, chunk)
    first_mix = jnp.einsum(
        "Jjb,sabc->Jsajc", mix_by_dest, inputs, preferred_element_type=f32
    ).astype(bf16)
    grad_unmixed = jnp.einsum(
        "qJj,saqc->Jsajc", unmix_by_dest, grad_values, preferred_element_type=f32
    ).astype(bf16)
    gate_weight = (
        inputs.astype(f32) * upstream * gate_sig * (1.0 + gate_pre * (1.0 - gate_sig))
    )
    weight_hi = gate_weight.astype(bf16)
    weight_lo = (gate_weight - weight_hi.astype(f32)).astype(bf16)
    gain_weight = jnp.einsum(
        "qJj,saqc->Jsajc", unmix_by_dest, weight_hi, preferred_element_type=f32
    ) + jnp.einsum("qJj,saqc->Jsajc", unmix_by_dest, weight_lo, preferred_element_type=f32)
    outgoing = jnp.stack([first_mix, grad_unmixed], axis=1)
    incoming = lax.all_to_all(outgoing, "seq", split_axis=0, concat_axis=0, tiled=True)
    incoming = jnp.moveaxis(incoming, 2, 1)
    spread_mix = incoming[:, :, 0].reshape(parts, scenes_here, local_a, chunk, channels)
    spread_grad = incoming[:, :, 1].reshape(parts, scenes_here, local_a, chunk, channels)
    spread_mix = jnp.moveaxis(spread_mix, 1, 0).reshape(scenes_here, parts * local_a, chunk, channels)
    spread_grad = jnp.moveaxis(spread_grad, 1, 0).reshape(
        scenes_here, parts * local_a, chunk, channels
    )

    second_mix = jnp.einsum(
        "ia,sajc->sijc", across_mix, spread_mix, preferred_element_type=f32
    ).astype(bf16)
    weighted = (second_mix.astype(f32) * kernel_f).astype(bf16)
    unmixed = jnp.einsum(
        "pi,sijc->spjc", across_unmix, weighted, preferred_element_type=f32
    ).astype(bf16)
    grad_weighted = jnp.einsum(
        "pi,spjc->sijc", across_unmix, spread_grad, preferred_element_type=f32
    )
    kernel_term = jnp.sum(grad_weighted * second_mix.astype(f32), axis=0)
    scene_parts = lax.axis_size("scene")
    inner = 4 if scene_parts % 4 == 0 else 1
    outer = scene_parts // inner
    scene_index = lax.axis_index("scene")
    outer_index = scene_index // inner
    inner_index = scene_index % inner
    term_by_dest = kernel_term.reshape(outer, inner, block_len // scene_parts, chunk, channels)
    term_sent = term_by_dest.astype(bf16)
    partial = lax.dynamic_index_in_dim(term_by_dest, outer_index, 0, False)
    for shift in range(1, outer):
        piece = lax.dynamic_index_in_dim(term_sent, (outer_index + shift) % outer, 0, False)
        pairs = [
            (o * inner + k, ((o + shift) % outer) * inner + k)
            for o in range(outer)
            for k in range(inner)
        ]
        partial = partial + lax.ppermute(piece, "scene", pairs).astype(f32)
    kernel_grad = lax.dynamic_index_in_dim(partial, inner_index, 0, False)
    partial_sent = partial.astype(bf16)
    for shift in range(1, inner):
        piece = lax.dynamic_index_in_dim(partial_sent, (inner_index + shift) % inner, 0, False)
        pairs = [
            (o * inner + k, o * inner + (k + shift) % inner)
            for o in range(outer)
            for k in range(inner)
        ]
        kernel_grad = kernel_grad + lax.ppermute(piece, "scene", pairs).astype(f32)
    grad_second = (grad_weighted * kernel_f).astype(bf16)
    grad_first = jnp.einsum(
        "ia,sijc->sajc", across_mix, grad_second, preferred_element_type=f32
    ).astype(bf16)
    back = jnp.stack(
        [
            unmixed.reshape(scenes_here, parts, local_a, chunk, channels),
            grad_first.reshape(scenes_here, parts, local_a, chunk, channels),
        ],
        axis=2,
    )
    back = jnp.moveaxis(back, 1, 0)
    returned = lax.all_to_all(back, "seq", split_axis=0, concat_axis=0, tiled=True)
    returned, kernel_grad = lax.optimization_barrier((returned, kernel_grad))
    values = jnp.einsum(
        "qJj,Jsajc->saqc",
        unmix_by_dest,
        returned[:, :, 0],
        preferred_element_type=f32,
    )
    mixed_out = (values * gate).astype(bf16).reshape(scenes_here, row_count, channels)
    grad_gate = upstream * values * gate_sig * (1.0 + gate_pre * (1.0 - gate_sig))
    grad_input = (
        jnp.einsum("Jjb,Jsajc->sabc", mix_by_dest, returned[:, :, 1], preferred_element_type=f32)
        + grad_gate * gate_gain
    )
    grad_input = grad_input.astype(bf16).reshape(scenes_here, row_count, channels)
    gain_term = jnp.sum(returned[:, :, 0].astype(f32) * gain_weight, axis=(0, 1, 2, 3))
    devices = lax.axis_size(("scene", "seq"))
    gain_spread = lax.all_to_all(
        jnp.broadcast_to(gain_term, (devices, channels)),
        ("scene", "seq"),
        split_axis=0,
        concat_axis=0,
        tiled=True,
    )
    gain_total = jnp.sum(gain_spread, axis=0)
    total_rows = scenes_here * lax.axis_size("scene") * local_a * parts * block_len
    grad_scale = 1.0 / jnp.sqrt(jnp.float32(total_rows))
    return (mixed_out, grad_input, kernel_grad, gain_total * grad_scale)


def solution(mesh):
    return jax.shard_map(
        on_device,
        mesh=mesh,
        in_specs=(
            P("scene", "seq", None),
            P("scene", "seq", None),
            P(),
            P(None, "seq", None),
            P(),
            P(),
            P(),
            P(),
        ),
        out_specs=(P("scene", "seq", None), P("scene", "seq", None), P("scene", "seq", None), P()),
        check_vma=False,
    )
```

```python
import jax
import jax.numpy as jnp
from jax import lax
from jax.sharding import PartitionSpec as P


def on_device(
    scene_x, cotangent, gate_gain, kernel, block_mix, across_mix, across_unmix, block_unmix
):
    f32 = jnp.float32
    bf16 = jnp.bfloat16
    scenes_here, row_count, channels = scene_x.shape
    block_len = block_mix.shape[0]
    local_a = row_count // block_len
    parts = lax.axis_size("seq")
    chunk = block_len // parts
    kernel_f = kernel.astype(f32)

    inputs = scene_x.reshape(scenes_here, local_a, block_len, channels)
    upstream = cotangent.reshape(scenes_here, local_a, block_len, channels).astype(f32)
    gate_pre = inputs.astype(f32) * gate_gain
    gate_sig = jax.nn.sigmoid(gate_pre)
    gate = gate_pre * gate_sig
    grad_values = (upstream * gate).astype(bf16)
    mix_by_dest = block_mix.reshape(parts, chunk, block_len)
    unmix_by_dest = block_unmix.reshape(block_len, parts, chunk)
    first_mix = jnp.einsum(
        "Jjb,sabc->Jsajc", mix_by_dest, inputs, preferred_element_type=f32
    ).astype(bf16)
    grad_unmixed = jnp.einsum(
        "qJj,saqc->Jsajc", unmix_by_dest, grad_values, preferred_element_type=f32
    ).astype(bf16)
    outgoing = jnp.stack([first_mix, grad_unmixed], axis=1)
    incoming = lax.all_to_all(outgoing, "seq", split_axis=0, concat_axis=0, tiled=True)
    incoming = jnp.moveaxis(incoming, 2, 1)
    spread_mix = incoming[:, :, 0].reshape(parts, scenes_here, local_a, chunk, channels)
    spread_grad = incoming[:, :, 1].reshape(parts, scenes_here, local_a, chunk, channels)
    spread_mix = jnp.moveaxis(spread_mix, 1, 0).reshape(scenes_here, parts * local_a, chunk, channels)
    spread_grad = jnp.moveaxis(spread_grad, 1, 0).reshape(
        scenes_here, parts * local_a, chunk, channels
    )

    second_mix = jnp.einsum(
        "ia,sajc->sijc", across_mix, spread_mix, preferred_element_type=f32
    ).astype(bf16)
    weighted = (second_mix.astype(f32) * kernel_f).astype(bf16)
    unmixed = jnp.einsum(
        "pi,sijc->spjc", across_unmix, weighted, preferred_element_type=f32
    ).astype(bf16)
    grad_weighted = jnp.einsum(
        "pi,spjc->sijc", across_unmix, spread_grad, preferred_element_type=f32
    )
    kernel_term = jnp.sum(grad_weighted * second_mix.astype(f32), axis=0)
    scene_parts = lax.axis_size("scene")
    inner = 4 if scene_parts % 4 == 0 else 1
    outer = scene_parts // inner
    scene_index = lax.axis_index("scene")
    outer_index = scene_index // inner
    inner_index = scene_index % inner
    term_by_dest = kernel_term.reshape(outer, inner, block_len // scene_parts, chunk, channels)
    term_sent = term_by_dest.astype(bf16)
    grad_second = (grad_weighted * kernel_f).astype(bf16)
    grad_first = jnp.einsum(
        "ia,sijc->sajc", across_mix, grad_second, preferred_element_type=f32
    ).astype(bf16)
    back = jnp.stack(
        [
            unmixed.reshape(scenes_here, parts, local_a, chunk, channels),
            grad_first.reshape(scenes_here, parts, local_a, chunk, channels),
        ],
        axis=2,
    )
    back = jnp.moveaxis(back, 1, 0)
    back, term_sent = lax.optimization_barrier((back, term_sent))
    partial = lax.dynamic_index_in_dim(term_by_dest, outer_index, 0, False)
    for shift in range(1, outer):
        piece = lax.dynamic_index_in_dim(term_sent, (outer_index + shift) % outer, 0, False)
        pairs = [
            (o * inner + k, ((o + shift) % outer) * inner + k)
            for o in range(outer)
            for k in range(inner)
        ]
        partial = partial + lax.ppermute(piece, "scene", pairs).astype(f32)
    kernel_grad = lax.dynamic_index_in_dim(partial, inner_index, 0, False)
    partial_sent = partial.astype(bf16)
    for shift in range(1, inner):
        piece = lax.dynamic_index_in_dim(partial_sent, (inner_index + shift) % inner, 0, False)
        pairs = [
            (o * inner + k, o * inner + (k + shift) % inner)
            for o in range(outer)
            for k in range(inner)
        ]
        kernel_grad = kernel_grad + lax.ppermute(piece, "scene", pairs).astype(f32)
    returned = lax.all_to_all(back, "seq", split_axis=0, concat_axis=0, tiled=True)
    values = jnp.einsum(
        "qJj,Jsajc->saqc",
        unmix_by_dest,
        returned[:, :, 0],
        preferred_element_type=f32,
    )
    mixed_out = (values * gate).astype(bf16).reshape(scenes_here, row_count, channels)
    grad_gate = upstream * values * gate_sig * (1.0 + gate_pre * (1.0 - gate_sig))
    grad_input = (
        jnp.einsum("Jjb,Jsajc->sabc", mix_by_dest, returned[:, :, 1], preferred_element_type=f32)
        + grad_gate * gate_gain
    )
    grad_input = grad_input.astype(bf16).reshape(scenes_here, row_count, channels)
    gain_term = jnp.sum(inputs.astype(f32) * grad_gate, axis=(0, 1, 2))
    devices = lax.axis_size(("scene", "seq"))
    gain_spread = lax.all_to_all(
        jnp.broadcast_to(gain_term, (devices, channels)),
        ("scene", "seq"),
        split_axis=0,
        concat_axis=0,
        tiled=True,
    )
    gain_total = jnp.sum(gain_spread, axis=0)
    total_rows = scenes_here * lax.axis_size("scene") * local_a * parts * block_len
    grad_scale = 1.0 / jnp.sqrt(jnp.float32(total_rows))
    return (mixed_out, grad_input, kernel_grad, gain_total * grad_scale)


def solution(mesh):
    return jax.shard_map(
        on_device,
        mesh=mesh,
        in_specs=(
            P("scene", "seq", None),
            P("scene", "seq", None),
            P(),
            P(None, "seq", None),
            P(),
            P(),
            P(),
            P(),
        ),
        out_specs=(P("scene", "seq", None), P("scene", "seq", None), P("scene", "seq", None), P()),
        check_vma=False,
    )
```

```python
import jax
import jax.numpy as jnp
from jax import lax
from jax.sharding import PartitionSpec as P


def on_device(
    scene_x, cotangent, gate_gain, kernel, block_mix, across_mix, across_unmix, block_unmix
):
    f32 = jnp.float32
    bf16 = jnp.bfloat16
    scenes_here, row_count, channels = scene_x.shape
    block_len = block_mix.shape[0]
    local_a = row_count // block_len
    parts = lax.axis_size("seq")
    chunk = block_len // parts
    kernel_f = kernel.astype(f32)

    inputs = scene_x.reshape(scenes_here, local_a, block_len, channels)
    upstream = cotangent.reshape(scenes_here, local_a, block_len, channels).astype(f32)
    gate_pre = inputs.astype(f32) * gate_gain
    gate_sig = jax.nn.sigmoid(gate_pre)
    gate = gate_pre * gate_sig
    grad_values = (upstream * gate).astype(bf16)
    mix_by_dest = block_mix.reshape(parts, chunk, block_len)
    unmix_by_dest = block_unmix.reshape(block_len, parts, chunk)
    first_mix = jnp.einsum(
        "Jjb,sabc->Jsajc", mix_by_dest, inputs, preferred_element_type=f32
    ).astype(bf16)
    grad_unmixed = jnp.einsum(
        "qJj,saqc->Jsajc", unmix_by_dest, grad_values, preferred_element_type=f32
    ).astype(bf16)
    outgoing = jnp.stack([first_mix, grad_unmixed], axis=1)
    incoming = lax.all_to_all(outgoing, "seq", split_axis=0, concat_axis=0, tiled=True)
    incoming = jnp.moveaxis(incoming, 2, 1)
    spread_mix = incoming[:, :, 0].reshape(parts, scenes_here, local_a, chunk, channels)
    spread_grad = incoming[:, :, 1].reshape(parts, scenes_here, local_a, chunk, channels)
    spread_mix = jnp.moveaxis(spread_mix, 1, 0).reshape(scenes_here, parts * local_a, chunk, channels)
    spread_grad = jnp.moveaxis(spread_grad, 1, 0).reshape(
        scenes_here, parts * local_a, chunk, channels
    )

    second_mix = jnp.einsum(
        "ia,sajc->sijc", across_mix, spread_mix, preferred_element_type=f32
    ).astype(bf16)
    weighted = (second_mix.astype(f32) * kernel_f).astype(bf16)
    unmixed = jnp.einsum(
        "pi,sijc->spjc", across_unmix, weighted, preferred_element_type=f32
    ).astype(bf16)
    grad_weighted = jnp.einsum(
        "pi,spjc->sijc", across_unmix, spread_grad, preferred_element_type=f32
    )
    kernel_term = jnp.sum(grad_weighted * second_mix.astype(f32), axis=0)
    scene_parts = lax.axis_size("scene")
    inner = 4 if scene_parts % 4 == 0 else 1
    outer = scene_parts // inner
    scene_index = lax.axis_index("scene")
    outer_index = scene_index // inner
    inner_index = scene_index % inner
    term_by_dest = kernel_term.reshape(outer, inner, block_len // scene_parts, chunk, channels)
    term_sent = term_by_dest.astype(bf16)
    partial = lax.dynamic_index_in_dim(term_by_dest, outer_index, 0, False)
    for shift in range(1, outer):
        piece = lax.dynamic_index_in_dim(term_sent, (outer_index + shift) % outer, 0, False)
        pairs = [
            (o * inner + k, ((o + shift) % outer) * inner + k)
            for o in range(outer)
            for k in range(inner)
        ]
        partial = partial + lax.ppermute(piece, "scene", pairs).astype(f32)
    kernel_grad = lax.dynamic_index_in_dim(partial, inner_index, 0, False)
    partial_sent = partial.astype(bf16)
    for shift in range(1, inner):
        piece = lax.dynamic_index_in_dim(partial_sent, (inner_index + shift) % inner, 0, False)
        pairs = [
            (o * inner + k, o * inner + (k + shift) % inner)
            for o in range(outer)
            for k in range(inner)
        ]
        kernel_grad = kernel_grad + lax.ppermute(piece, "scene", pairs).astype(f32)
    grad_second = (grad_weighted * kernel_f).astype(bf16)
    grad_first = jnp.einsum(
        "ia,sijc->sajc", across_mix, grad_second, preferred_element_type=f32
    ).astype(bf16)
    back = jnp.stack(
        [
            unmixed.reshape(scenes_here, parts, local_a, chunk, channels),
            grad_first.reshape(scenes_here, parts, local_a, chunk, channels),
        ],
        axis=2,
    )
    back = jnp.moveaxis(back, 1, 0)
    returned = lax.all_to_all(back, "seq", split_axis=0, concat_axis=0, tiled=True)
    values = jnp.einsum(
        "qJj,Jsajc->saqc",
        unmix_by_dest,
        returned[:, :, 0],
        preferred_element_type=f32,
    )
    mixed_out = (values * gate).astype(bf16).reshape(scenes_here, row_count, channels)
    grad_gate = upstream * values * gate_sig * (1.0 + gate_pre * (1.0 - gate_sig))
    grad_input = (
        jnp.einsum("Jjb,Jsajc->sabc", mix_by_dest, returned[:, :, 1], preferred_element_type=f32)
        + grad_gate * gate_gain
    )
    grad_input = grad_input.astype(bf16).reshape(scenes_here, row_count, channels)
    gain_term = jnp.sum(inputs.astype(f32) * grad_gate, axis=(0, 1, 2))
    devices = lax.axis_size(("seq", "scene"))
    gain_spread = lax.all_to_all(
        jnp.broadcast_to(gain_term, (devices, channels)),
        ("seq", "scene"),
        split_axis=0,
        concat_axis=0,
        tiled=True,
    )
    gain_total = jnp.sum(gain_spread, axis=0)
    total_rows = scenes_here * lax.axis_size("scene") * local_a * parts * block_len
    grad_scale = 1.0 / jnp.sqrt(jnp.float32(total_rows))
    return (mixed_out, grad_input, kernel_grad, gain_total * grad_scale)


def solution(mesh):
    return jax.shard_map(
        on_device,
        mesh=mesh,
        in_specs=(
            P("scene", "seq", None),
            P("scene", "seq", None),
            P(),
            P(None, "seq", None),
            P(),
            P(),
            P(),
            P(),
        ),
        out_specs=(P("scene", "seq", None), P("scene", "seq", None), P("scene", "seq", None), P()),
        check_vma=False,
    )
```

```python
import jax
import jax.numpy as jnp
from jax import lax
from jax.sharding import PartitionSpec as P


def on_device(
    scene_x, cotangent, gate_gain, kernel, block_mix, across_mix, across_unmix, block_unmix
):
    f32 = jnp.float32
    bf16 = jnp.bfloat16
    scenes_here, row_count, channels = scene_x.shape
    block_len = block_mix.shape[0]
    local_a = row_count // block_len
    parts = lax.axis_size("seq")
    chunk = block_len // parts
    kernel_f = kernel.astype(f32)

    inputs = scene_x.reshape(scenes_here, local_a, block_len, channels)
    upstream = cotangent.reshape(scenes_here, local_a, block_len, channels).astype(f32)
    gate_pre = inputs.astype(f32) * gate_gain
    gate_sig = jax.nn.sigmoid(gate_pre)
    gate = gate_pre * gate_sig
    grad_values = (upstream * gate).astype(bf16)
    mix_by_dest = block_mix.reshape(parts, chunk, block_len)
    unmix_by_dest = block_unmix.reshape(block_len, parts, chunk)
    first_mix = jnp.einsum(
        "Jjb,sabc->Jsajc", mix_by_dest, inputs, preferred_element_type=f32
    ).astype(bf16)
    grad_unmixed = jnp.einsum(
        "qJj,saqc->Jsajc", unmix_by_dest, grad_values, preferred_element_type=f32
    ).astype(bf16)
    gate_weight = (
        inputs.astype(f32) * upstream * gate_sig * (1.0 + gate_pre * (1.0 - gate_sig))
    )
    weight_hi = gate_weight.astype(bf16)
    weight_lo = (gate_weight - weight_hi.astype(f32)).astype(bf16)
    gain_weight = jnp.einsum(
        "qJj,saqc->Jsajc", unmix_by_dest, weight_hi, preferred_element_type=f32
    ) + jnp.einsum("qJj,saqc->Jsajc", unmix_by_dest, weight_lo, preferred_element_type=f32)
    outgoing = jnp.stack([first_mix, grad_unmixed], axis=1)
    incoming = lax.all_to_all(outgoing, "seq", split_axis=0, concat_axis=0, tiled=True)
    incoming = jnp.moveaxis(incoming, 2, 1)
    spread_mix = incoming[:, :, 0].reshape(parts, scenes_here, local_a, chunk, channels)
    spread_grad = incoming[:, :, 1].reshape(parts, scenes_here, local_a, chunk, channels)
    spread_mix = jnp.moveaxis(spread_mix, 1, 0).reshape(scenes_here, parts * local_a, chunk, channels)
    spread_grad = jnp.moveaxis(spread_grad, 1, 0).reshape(
        scenes_here, parts * local_a, chunk, channels
    )

    second_mix = jnp.einsum(
        "ia,sajc->sijc", across_mix, spread_mix, preferred_element_type=f32
    ).astype(bf16)
    weighted = (second_mix.astype(f32) * kernel_f).astype(bf16)
    unmixed = jnp.einsum(
        "pi,sijc->spjc", across_unmix, weighted, preferred_element_type=f32
    ).astype(bf16)
    grad_weighted = jnp.einsum(
        "pi,spjc->sijc", across_unmix, spread_grad, preferred_element_type=f32
    )
    kernel_term = jnp.sum(grad_weighted * second_mix.astype(f32), axis=0)
    scene_parts = lax.axis_size("scene")
    inner = 4 if scene_parts % 4 == 0 else 1
    outer = scene_parts // inner
    scene_index = lax.axis_index("scene")
    outer_index = scene_index // inner
    inner_index = scene_index % inner
    term_by_dest = kernel_term.reshape(outer, inner, block_len // scene_parts, chunk, channels)
    term_sent = term_by_dest.astype(bf16)
    partial = lax.dynamic_index_in_dim(term_by_dest, outer_index, 0, False)
    for shift in range(1, outer):
        piece = lax.dynamic_index_in_dim(term_sent, (outer_index + shift) % outer, 0, False)
        pairs = [
            (o * inner + k, ((o + shift) % outer) * inner + k)
            for o in range(outer)
            for k in range(inner)
        ]
        partial = partial + lax.ppermute(piece, "scene", pairs).astype(f32)
    kernel_grad = lax.dynamic_index_in_dim(partial, inner_index, 0, False)
    partial_sent = partial.astype(bf16)
    stage_two = []
    for shift in range(1, inner):
        piece = lax.dynamic_index_in_dim(partial_sent, (inner_index + shift) % inner, 0, False)
        pairs = [
            (o * inner + k, o * inner + (k + shift) % inner)
            for o in range(outer)
            for k in range(inner)
        ]
        stage_two.append(lax.ppermute(piece, "scene", pairs))
    grad_second = (grad_weighted * kernel_f).astype(bf16)
    grad_first = jnp.einsum(
        "ia,sijc->sajc", across_mix, grad_second, preferred_element_type=f32
    ).astype(bf16)
    back = jnp.stack(
        [
            unmixed.reshape(scenes_here, parts, local_a, chunk, channels),
            grad_first.reshape(scenes_here, parts, local_a, chunk, channels),
        ],
        axis=2,
    )
    back = jnp.moveaxis(back, 1, 0)
    returned = lax.all_to_all(back, "seq", split_axis=0, concat_axis=0, tiled=True)
    values = jnp.einsum(
        "qJj,Jsajc->saqc",
        unmix_by_dest,
        returned[:, :, 0],
        preferred_element_type=f32,
    )
    mixed_out = (values * gate).astype(bf16).reshape(scenes_here, row_count, channels)
    grad_gate = upstream * values * gate_sig * (1.0 + gate_pre * (1.0 - gate_sig))
    grad_input = (
        jnp.einsum("Jjb,Jsajc->sabc", mix_by_dest, returned[:, :, 1], preferred_element_type=f32)
        + grad_gate * gate_gain
    )
    grad_input = grad_input.astype(bf16).reshape(scenes_here, row_count, channels)
    gain_term = jnp.sum(returned[:, :, 0].astype(f32) * gain_weight, axis=(0, 1, 2, 3))
    mixed_out, grad_input, stage_two = lax.optimization_barrier((mixed_out, grad_input, stage_two))
    for moved in stage_two:
        kernel_grad = kernel_grad + moved.astype(f32)
    gain_term, kernel_grad = lax.optimization_barrier((gain_term, kernel_grad))
    devices = lax.axis_size(("scene", "seq"))
    gain_spread = lax.all_to_all(
        jnp.broadcast_to(gain_term, (devices, channels)),
        ("scene", "seq"),
        split_axis=0,
        concat_axis=0,
        tiled=True,
    )
    gain_total = jnp.sum(gain_spread, axis=0)
    total_rows = scenes_here * lax.axis_size("scene") * local_a * parts * block_len
    grad_scale = 1.0 / jnp.sqrt(jnp.float32(total_rows))
    return (mixed_out, grad_input, kernel_grad, gain_total * grad_scale)


def solution(mesh):
    return jax.shard_map(
        on_device,
        mesh=mesh,
        in_specs=(
            P("scene", "seq", None),
            P("scene", "seq", None),
            P(),
            P(None, "seq", None),
            P(),
            P(),
            P(),
            P(),
        ),
        out_specs=(P("scene", "seq", None), P("scene", "seq", None), P("scene", "seq", None), P()),
        check_vma=False,
    )
```

```python
import jax
import jax.numpy as jnp
from jax import lax
from jax.sharding import PartitionSpec as P


def on_device(
    scene_x, cotangent, gate_gain, kernel, block_mix, across_mix, across_unmix, block_unmix
):
    f32 = jnp.float32
    bf16 = jnp.bfloat16
    scenes_here, row_count, channels = scene_x.shape
    block_len = block_mix.shape[0]
    local_a = row_count // block_len
    parts = lax.axis_size("seq")
    chunk = block_len // parts
    kernel_f = kernel.astype(f32)

    inputs = scene_x.reshape(scenes_here, local_a, block_len, channels)
    upstream = cotangent.reshape(scenes_here, local_a, block_len, channels).astype(f32)
    gate_pre = inputs.astype(f32) * gate_gain
    gate_sig = jax.nn.sigmoid(gate_pre)
    gate = gate_pre * gate_sig
    grad_values = (upstream * gate).astype(bf16)
    mix_by_dest = block_mix.reshape(parts, chunk, block_len)
    unmix_by_dest = block_unmix.reshape(block_len, parts, chunk)
    first_mix = jnp.einsum(
        "Jjb,sabc->Jsajc", mix_by_dest, inputs, preferred_element_type=f32
    ).astype(bf16)
    grad_unmixed = jnp.einsum(
        "qJj,saqc->Jsajc", unmix_by_dest, grad_values, preferred_element_type=f32
    ).astype(bf16)
    outgoing = jnp.stack([first_mix, grad_unmixed], axis=1)
    incoming = lax.all_to_all(outgoing, "seq", split_axis=0, concat_axis=0, tiled=True)
    incoming = jnp.moveaxis(incoming, 2, 1)
    spread_mix = incoming[:, :, 0].reshape(parts, scenes_here, local_a, chunk, channels)
    spread_grad = incoming[:, :, 1].reshape(parts, scenes_here, local_a, chunk, channels)
    spread_mix = jnp.moveaxis(spread_mix, 1, 0).reshape(scenes_here, parts * local_a, chunk, channels)
    spread_grad = jnp.moveaxis(spread_grad, 1, 0).reshape(
        scenes_here, parts * local_a, chunk, channels
    )

    second_mix = jnp.einsum(
        "ia,sajc->sijc", across_mix, spread_mix, preferred_element_type=f32
    ).astype(bf16)
    weighted = (second_mix.astype(f32) * kernel_f).astype(bf16)
    unmixed = jnp.einsum(
        "pi,sijc->spjc", across_unmix, weighted, preferred_element_type=f32
    ).astype(bf16)
    grad_weighted = jnp.einsum(
        "pi,spjc->sijc", across_unmix, spread_grad, preferred_element_type=f32
    )
    kernel_term = jnp.sum(grad_weighted * second_mix.astype(f32), axis=0)
    scene_parts = lax.axis_size("scene")
    inner = 4 if scene_parts % 4 == 0 else 1
    outer = scene_parts // inner
    scene_index = lax.axis_index("scene")
    outer_index = scene_index % outer
    inner_index = scene_index // outer
    term_by_dest = kernel_term.reshape(inner, outer, block_len // scene_parts, chunk, channels)
    term_by_dest = jnp.swapaxes(term_by_dest, 0, 1)
    term_sent = term_by_dest.astype(bf16)
    partial = lax.dynamic_index_in_dim(term_by_dest, outer_index, 0, False)
    for shift in range(1, outer):
        piece = lax.dynamic_index_in_dim(term_sent, (outer_index + shift) % outer, 0, False)
        pairs = [
            (k * outer + o, k * outer + (o + shift) % outer)
            for o in range(outer)
            for k in range(inner)
        ]
        partial = partial + lax.ppermute(piece, "scene", pairs).astype(f32)
    kernel_grad = lax.dynamic_index_in_dim(partial, inner_index, 0, False)
    partial_sent = partial.astype(bf16)
    for shift in range(1, inner):
        piece = lax.dynamic_index_in_dim(partial_sent, (inner_index + shift) % inner, 0, False)
        pairs = [
            (k * outer + o, ((k + shift) % inner) * outer + o)
            for o in range(outer)
            for k in range(inner)
        ]
        kernel_grad = kernel_grad + lax.ppermute(piece, "scene", pairs).astype(f32)
    grad_second = (grad_weighted * kernel_f).astype(bf16)
    grad_first = jnp.einsum(
        "ia,sijc->sajc", across_mix, grad_second, preferred_element_type=f32
    ).astype(bf16)
    back = jnp.stack(
        [
            unmixed.reshape(scenes_here, parts, local_a, chunk, channels),
            grad_first.reshape(scenes_here, parts, local_a, chunk, channels),
        ],
        axis=2,
    )
    back = jnp.moveaxis(back, 1, 0)
    returned = lax.all_to_all(back, "seq", split_axis=0, concat_axis=0, tiled=True)
    values = jnp.einsum(
        "qJj,Jsajc->saqc",
        unmix_by_dest,
        returned[:, :, 0],
        preferred_element_type=f32,
    )
    mixed_out = (values * gate).astype(bf16).reshape(scenes_here, row_count, channels)
    grad_gate = upstream * values * gate_sig * (1.0 + gate_pre * (1.0 - gate_sig))
    grad_input = (
        jnp.einsum("Jjb,Jsajc->sabc", mix_by_dest, returned[:, :, 1], preferred_element_type=f32)
        + grad_gate * gate_gain
    )
    grad_input = grad_input.astype(bf16).reshape(scenes_here, row_count, channels)
    gain_term = jnp.sum(inputs.astype(f32) * grad_gate, axis=(0, 1, 2))
    devices = lax.axis_size(("scene", "seq"))
    gain_spread = lax.all_to_all(
        jnp.broadcast_to(gain_term, (devices, channels)),
        ("scene", "seq"),
        split_axis=0,
        concat_axis=0,
        tiled=True,
    )
    gain_total = jnp.sum(gain_spread, axis=0)
    total_rows = scenes_here * lax.axis_size("scene") * local_a * parts * block_len
    grad_scale = 1.0 / jnp.sqrt(jnp.float32(total_rows))
    return (mixed_out, grad_input, kernel_grad, gain_total * grad_scale)


def solution(mesh):
    return jax.shard_map(
        on_device,
        mesh=mesh,
        in_specs=(
            P("scene", "seq", None),
            P("scene", "seq", None),
            P(),
            P(None, "seq", None),
            P(),
            P(),
            P(),
            P(),
        ),
        out_specs=(P("scene", "seq", None), P("scene", "seq", None), P("scene", "seq", None), P()),
        check_vma=False,
    )
```
